768 devices in a mesh: wave: 48 (over x, z), lev: 16 (over y, core).
Axes of the slice: x: 4, y: 8, z: 12, core: 2. Of those that a mesh axis runs over, the one named last changes fastest.
Arguments:
- spectral: bfloat16 [96, 768, 1280], P('lev', 'wave'), may hold values from -0.19921875 to 0.19921875
- legendre: bfloat16 [768, 768, 1280], P('wave', 'lev'), may hold values from -0.15625 to 0.15625
- weights: float32 [768], replicated, may hold values from 4 to 40
- nlon: int32 [768], replicated, may hold values from 20 to 5136, as said below
- assignment: int32 [768], replicated, may hold values from 1 to 1279, as said below
Outputs:
- tendencies: float32 [96, 768, 1280], P('lev', 'wave')
The draws below stay inside these ranges and needn't reach their ends.
Inputs may be any that keep to these rules, and one draw needn't show every extreme that they name: `assignment`: slots 2 i and 2 i + 1 hold m and 1280 - m for some m with 1 <= m < 640; all values are distinct, and m = 1 is always among them. `nlon`: each count is 20 plus four times a whole number; both ends of the range occur in every draw.
All inputs are finite; a program needn't handle non-finite values.
Results may differ from the reference program's by a relative error of at most 0.018.
Values may be sent and summed in bfloat16 or wider, within the bound.
No kernel may reach another device: no remote copies, remote signals or barrier semaphores. Data moves between devices by JAX's collectives and lax.ppermute only.
A program may use at most 32 MiB of HBM per device.

```python
import math
import jax
import jax.numpy as jnp
from jax import lax

TRUNC = 1279
KMAX = 1280
MW = 768
COLS = 96
LAT = 768
NLONPAD = 5376
N_WAVE = 48
N_LEV = 16


def draw_assignment(key, part):
    half_count = MW // 2
    pool = jax.random.permutation(key, (TRUNC + 1) // 2 - 1)[:half_count] + 1
    pool = pool.astype(jnp.int32)
    has_one = jnp.any(pool == 1)
    pool = jnp.where(has_one, pool, pool.at[0].set(1))
    second = (TRUNC + 1 - pool).astype(jnp.int32)
    return jnp.stack([pool, second], axis=1).reshape(MW).astype(jnp.int32)


def draw_nlon(key, part):
    first_key, second_key = jax.random.split(jax.random.fold_in(key, 17))
    counts = jax.random.randint(first_key, (LAT,), 0, TRUNC + 1)
    spots = jax.random.permutation(second_key, LAT)
    counts = counts.at[spots[0]].set(TRUNC).at[spots[1]].set(0)
    return (20 + 4 * counts).astype(jnp.int32)


def level_of(stream_key, extent, pieces, least, high):
    factor_of, own = 1.0, jax.random.fold_in(stream_key, 6)
    for axis_at, shards_of in pieces:
        draws = jnp.exp(jax.random.uniform(jax.random.fold_in(own, axis_at), (shards_of,), jnp.float32, least / len(pieces), high / len(pieces)))
        factor_of = factor_of * jnp.repeat(draws, extent[axis_at] // shards_of).reshape([-1 if axis == axis_at else 1 for axis in range(len(extent))])
    return factor_of


def gaussian(key, shape, scale, limit, shards=(), dtype=jnp.bfloat16):
    drawn = scale * jax.random.normal(key, shape, jnp.float32)
    if shards:
        drawn = drawn * level_of(key, shape, shards, -0.22, 0.18)
    return jnp.clip(drawn, -limit, limit).astype(dtype)


def setup_inputs(seed: int = 0) -> dict:
    key_of = jax.random.split(jax.random.key(seed), 6)
    return {
        "spectral": gaussian(key_of[0], (COLS, MW, KMAX), 0.03, 0.19921875, ((0, 16), (1, 48))),
        "legendre": gaussian(key_of[1], (MW, LAT, KMAX), KMAX ** -0.5, 0.15625, ((0, 48), (1, 16))),
        "weights": jnp.clip(jnp.exp(jax.random.uniform(key_of[2], (LAT,), jnp.float32, math.log(4.0), math.log(40.0))), 4.0, 40.0),
        "nlon": draw_nlon(jax.random.fold_in(key_of[5], 71), 0),
        "assignment": draw_assignment(jax.random.fold_in(key_of[5], 71), 0),
    }


def trig_table(count, waves, lon_rows):
    lon_col = lon_rows[:, None]
    phase = (lon_col * waves[None, :]) % count
    angle = (2.0 * math.pi) * phase.astype(jnp.float32) / count.astype(jnp.float32)
    usable = (lon_col < count) & (2 * waves[None, :] < count)
    cosine = jnp.where(usable, jnp.cos(angle), jnp.zeros((), jnp.float32))
    sine = jnp.where(usable, -jnp.sin(angle), jnp.zeros((), jnp.float32))
    return jnp.concatenate([cosine, sine], axis=1).astype(jnp.bfloat16)


def quadratic(grid):
    fields = grid.reshape(grid.shape[0], grid.shape[1] // 3, 3)
    vort = fields[:, :, 0]
    diverg = fields[:, :, 1]
    temper = fields[:, :, 2]
    stacked = jnp.stack([vort * temper, diverg * temper, vort * diverg], axis=-1)
    return stacked.reshape(grid.shape[0], grid.shape[1]).astype(jnp.bfloat16)


def reference(spectral, legendre, weights, nlon, assignment):
    krange = lax.iota(jnp.int32, KMAX)
    live_rows = krange[None, :] <= (TRUNC - assignment)[:, None]
    coeffs = jnp.where(live_rows[None], spectral, jnp.zeros((), jnp.bfloat16))
    by_slot = jnp.transpose(coeffs, (1, 0, 2))

    def synth_one(inputs):
        table_slot, coeff_slot = inputs
        return jnp.dot(table_slot, coeff_slot.T, preferred_element_type=jnp.float32).astype(jnp.bfloat16)

    fourier = lax.map(synth_one, (legendre, by_slot))
    lon_rows = lax.iota(jnp.int32, NLONPAD)
    half_cols = COLS // 2

    def grid_one(inputs):
        four_lat, count, weight = inputs
        pairs = four_lat.reshape(MW, half_cols, 2)
        stacked = jnp.concatenate([pairs[:, :, 0], pairs[:, :, 1]], axis=0)
        table = trig_table(count, assignment, lon_rows)
        grid = 2.0 * jnp.dot(table, stacked, preferred_element_type=jnp.float32)
        products = quadratic(grid)
        back = jnp.dot(table.T, products, preferred_element_type=jnp.float32)
        back = back * (weight / count.astype(jnp.float32))
        joined = jnp.stack([back[:MW], back[MW:]], axis=-1).reshape(MW, COLS)
        return joined.astype(jnp.bfloat16)

    analysed = lax.map(grid_one, (jnp.transpose(fourier, (1, 0, 2)), nlon, weights))
    analysed = jnp.transpose(analysed, (1, 0, 2))

    def direct_one(inputs):
        table_slot, anal_slot, wave = inputs
        bands_table = table_slot.reshape(N_LEV, N_WAVE, KMAX).astype(jnp.float32)
        bands_anal = anal_slot.reshape(N_LEV, N_WAVE, COLS).astype(jnp.float32)
        band_term = jnp.einsum("blc,blk->bck", bands_anal, bands_table)
        band_term = jnp.where((krange <= TRUNC - wave)[None, None, :], band_term, jnp.zeros((), jnp.float32))
        rounded = lax.optimization_barrier(band_term.astype(jnp.bfloat16))
        return jnp.sum(rounded.astype(jnp.float32), axis=0)

    result = lax.map(direct_one, (legendre, analysed, assignment))
    return jnp.transpose(result, (1, 0, 2))
```

```python
import math

import jax
import jax.numpy as jnp
from jax import lax
from jax.sharding import PartitionSpec as P

TRUNC = 1279
LON_BLOCK = 768
NLONPAD = 5376


def angle_parts(count, waves, starts):
    phase = starts[:, None] % count * waves[None, :] % count
    angle = 2.0 * math.pi * phase.astype(jnp.float32) / count.astype(jnp.float32)
    return (jnp.cos(angle), jnp.sin(angle))


def compose_table(count, waves, coarse_cos, coarse_sin, fine_cos, fine_sin, lon_rows):
    cosine = (
        coarse_cos[:, None, :] * fine_cos[None, :, :]
        - coarse_sin[:, None, :] * fine_sin[None, :, :]
    )
    sine = (
        coarse_sin[:, None, :] * fine_cos[None, :, :]
        + coarse_cos[:, None, :] * fine_sin[None, :, :]
    )
    rows_total = lon_rows.shape[0]
    cosine = cosine.reshape(rows_total, waves.shape[0])
    sine = sine.reshape(rows_total, waves.shape[0])
    usable = (lon_rows[:, None] < count) & (2 * waves[None, :] < count)
    cosine = jnp.where(usable, cosine, jnp.zeros((), jnp.float32))
    sine = jnp.where(usable, -sine, jnp.zeros((), jnp.float32))
    return jnp.concatenate([cosine, sine], axis=1).astype(jnp.bfloat16)


def quadratic(grid):
    fields = grid.reshape(grid.shape[0], grid.shape[1] // 3, 3)
    vort = fields[:, :, 0]
    diverg = fields[:, :, 1]
    temper = fields[:, :, 2]
    stacked = jnp.stack([vort * temper, diverg * temper, vort * diverg], axis=-1)
    return stacked.reshape(grid.shape[0], grid.shape[1]).astype(jnp.bfloat16)


def per_device(spectral, legendre, weights, nlon, assignment):
    wave_index = lax.axis_index("wave")
    lev_index = lax.axis_index("lev")
    slots = legendre.shape[0]
    lat_band = legendre.shape[1]
    kmax_width = legendre.shape[2]
    all_slots = assignment.shape[0]
    pairs_n = slots // 2
    own_waves = lax.dynamic_slice_in_dim(assignment, wave_index * slots, slots)
    krange = lax.iota(jnp.int32, kmax_width)
    front = krange[None, :] < (kmax_width - own_waves.reshape(pairs_n, 2)[:, 0])[:, None]
    leg_pairs = legendre.reshape(pairs_n, 2, lat_band, kmax_width)
    zero_bf = jnp.zeros((), jnp.bfloat16)
    leg_a = jnp.where(front[:, None, :], leg_pairs[:, 0], zero_bf)
    leg_b = jnp.where(front[:, None, :], zero_bf, leg_pairs[:, 1, :, ::-1])
    packed_leg = jnp.stack([leg_a, leg_b], axis=1)
    spec_pairs = spectral.reshape(spectral.shape[0], pairs_n, 2, kmax_width)
    packed_spec = jnp.where(front[None], spec_pairs[:, :, 0], spec_pairs[:, :, 1, ::-1])
    spec_all = lax.all_gather(packed_spec, "lev", axis=0, tiled=True)
    columns = spec_all.shape[0]
    four_local = jnp.einsum(
        "pxlk,cpk->pxlc", packed_leg, spec_all, preferred_element_type=jnp.float32
    ).astype(jnp.bfloat16).reshape(slots, lat_band, columns)
    fourier = lax.all_to_all(four_local, "wave", split_axis=1, concat_axis=0, tiled=True)
    mine = fourier.shape[1]
    half_cols = columns // 2
    fine_rows = lax.iota(jnp.int32, 128)
    coarse_rows = lax.iota(jnp.int32, NLONPAD // 128) * 128
    coarse_step = LON_BLOCK // 128
    lat_index = lev_index * lat_band + wave_index * mine + 0
    count = lax.dynamic_slice_in_dim(nlon, lat_index, 1)[0]
    weight = lax.dynamic_slice_in_dim(weights, lat_index, 1)[0]
    pairs = fourier[:, 0, :].reshape(all_slots, half_cols, 2)
    stacked = jnp.concatenate([pairs[:, :, 0], pairs[:, :, 1]], axis=0)
    fine_cos, fine_sin = angle_parts(count, assignment, fine_rows)
    coarse_cos_all, coarse_sin_all = angle_parts(count, assignment, coarse_rows)

    def lon_block(block_step, total):
        lon_rows = block_step * LON_BLOCK + lax.iota(jnp.int32, LON_BLOCK)
        coarse_cos = lax.dynamic_slice_in_dim(coarse_cos_all, block_step * coarse_step, coarse_step)
        coarse_sin = lax.dynamic_slice_in_dim(coarse_sin_all, block_step * coarse_step, coarse_step)
        table = compose_table(
            count, assignment, coarse_cos, coarse_sin, fine_cos, fine_sin, lon_rows
        )
        grid = 2.0 * jnp.dot(table, stacked, preferred_element_type=jnp.float32)
        products = quadratic(grid)
        return total + lax.dot_general(
            table, products, (((0,), (0,)), ((), ())), preferred_element_type=jnp.float32
        )

    start_total = jnp.zeros((2 * all_slots, half_cols), jnp.float32)
    total = lax.fori_loop(0, NLONPAD // LON_BLOCK, lon_block, start_total)
    back = total * (weight / count.astype(jnp.float32))
    joined = jnp.stack([back[:all_slots], back[all_slots:]], axis=-1).reshape(all_slots, columns)
    analysed_rows = [joined.astype(jnp.bfloat16)]
    analysed = jnp.stack(analysed_rows, axis=1)
    returned = lax.all_to_all(analysed, "wave", split_axis=0, concat_axis=1, tiled=True)
    returned = returned.reshape(pairs_n, 2, lat_band, columns)
    band_term = jnp.einsum(
        "pxlc,pxlk->cpk", returned, packed_leg, preferred_element_type=jnp.float32
    )
    summed = lax.psum_scatter(
        band_term.astype(jnp.bfloat16), "lev", scatter_dimension=0, tiled=True
    )
    zero_f = jnp.zeros((), jnp.float32)
    summed = summed.astype(jnp.float32)
    out_a = jnp.where(front[None], summed, zero_f)
    out_b = jnp.where(front[None], zero_f, summed)[:, :, ::-1]
    out = jnp.stack([out_a, out_b], axis=2)
    return out.reshape(summed.shape[0], slots, kmax_width)


def solution(mesh):
    return jax.shard_map(
        per_device,
        mesh=mesh,
        in_specs=(P("lev", "wave", None), P("wave", "lev", None), P(), P(), P()),
        out_specs=P("lev", "wave", None),
        check_vma=False,
    )
```

```python
import math

import jax
import jax.numpy as jnp
from jax import lax
from jax.sharding import PartitionSpec as P

TRUNC = 1279
LON_BLOCK = 768
NLONPAD = 5376


def angle_parts(count, waves, starts):
    phase = starts[:, None] % count * waves[None, :] % count
    angle = 2.0 * math.pi * phase.astype(jnp.float32) / count.astype(jnp.float32)
    return (jnp.cos(angle), jnp.sin(angle))


def compose_table(row_limit, count, waves, coarse_cos, coarse_sin, fine_cos, fine_sin, lon_rows):
    cosine = (
        coarse_cos[:, None, :] * fine_cos[None, :, :]
        - coarse_sin[:, None, :] * fine_sin[None, :, :]
    )
    sine = (
        coarse_sin[:, None, :] * fine_cos[None, :, :]
        + coarse_cos[:, None, :] * fine_sin[None, :, :]
    )
    rows_total = lon_rows.shape[0]
    cosine = cosine.reshape(rows_total, waves.shape[0])
    sine = sine.reshape(rows_total, waves.shape[0])
    usable = (lon_rows[:, None] < row_limit) & (2 * waves[None, :] < count)
    cosine = jnp.where(usable, cosine, jnp.zeros((), jnp.float32))
    sine = jnp.where(usable, -sine, jnp.zeros((), jnp.float32))
    return jnp.concatenate([cosine, sine], axis=1).astype(jnp.bfloat16)


def quadratic(grid):
    fields = grid.reshape(grid.shape[0], grid.shape[1] // 3, 3)
    vort = fields[:, :, 0]
    diverg = fields[:, :, 1]
    temper = fields[:, :, 2]
    stacked = jnp.stack([vort * temper, diverg * temper, vort * diverg], axis=-1)
    return stacked.reshape(grid.shape[0], grid.shape[1]).astype(jnp.bfloat16)


def per_device(spectral, legendre, weights, nlon, assignment):
    wave_index = lax.axis_index("wave")
    lev_index = lax.axis_index("lev")
    slots = legendre.shape[0]
    lat_band = legendre.shape[1]
    kmax_width = legendre.shape[2]
    all_slots = assignment.shape[0]
    pairs_n = slots // 2
    own_waves = lax.dynamic_slice_in_dim(assignment, wave_index * slots, slots)
    krange = lax.iota(jnp.int32, kmax_width)
    front = krange[None, :] < (kmax_width - own_waves.reshape(pairs_n, 2)[:, 0])[:, None]
    leg_pairs = legendre.reshape(pairs_n, 2, lat_band, kmax_width)
    zero_bf = jnp.zeros((), jnp.bfloat16)
    leg_a = jnp.where(front[:, None, :], leg_pairs[:, 0], zero_bf)
    leg_b = jnp.where(front[:, None, :], zero_bf, leg_pairs[:, 1, :, ::-1])
    packed_leg = jnp.stack([leg_a, leg_b], axis=1)
    spec_pairs = spectral.reshape(spectral.shape[0], pairs_n, 2, kmax_width)
    packed_spec = jnp.where(front[None], spec_pairs[:, :, 0], spec_pairs[:, :, 1, ::-1])
    spec_all = lax.all_gather(packed_spec, "lev", axis=0, tiled=True)
    columns = spec_all.shape[0]
    four_local = jnp.einsum(
        "pxlk,cpk->pxlc", packed_leg, spec_all, preferred_element_type=jnp.float32
    ).astype(jnp.bfloat16).reshape(slots, lat_band, columns)
    fourier = lax.all_to_all(four_local, "wave", split_axis=1, concat_axis=0, tiled=True)
    mine = fourier.shape[1]
    half_cols = columns // 2
    lat_index = lev_index * lat_band + wave_index * mine + 0
    count = lax.dynamic_slice_in_dim(nlon, lat_index, 1)[0]
    weight = lax.dynamic_slice_in_dim(weights, lat_index, 1)[0]
    half_rows = NLONPAD // 2
    half = count // 2
    fine_rows = lax.iota(jnp.int32, 128)
    coarse_rows = lax.iota(jnp.int32, half_rows // 128) * 128
    lon_rows = lax.iota(jnp.int32, half_rows)
    fine_cos, fine_sin = angle_parts(count, assignment, fine_rows)
    coarse_cos, coarse_sin = angle_parts(count, assignment, coarse_rows)
    table = compose_table(
        half + 1, count, assignment, coarse_cos, coarse_sin, fine_cos, fine_sin, lon_rows
    )
    pairs = fourier[:, 0, :].reshape(all_slots, half_cols, 2)
    zero_bf = jnp.zeros((), jnp.bfloat16)
    blank = jnp.zeros((all_slots, half_cols), jnp.bfloat16)
    split = jnp.concatenate(
        [
            jnp.concatenate([pairs[:, :, 0], blank], axis=1),
            jnp.concatenate([blank, pairs[:, :, 1]], axis=1),
        ],
        axis=0,
    )
    parts = jnp.dot(table, split, preferred_element_type=jnp.float32)
    even, odd = parts[:, :half_cols], parts[:, half_cols:]
    grid_pos = 2.0 * (even + odd)
    grid_neg = 2.0 * (even - odd)
    mirrored = (lon_rows > 0) & (lon_rows < half)
    prod_pos = quadratic(grid_pos)
    prod_neg = jnp.where(mirrored[:, None], quadratic(grid_neg), zero_bf)
    both = jnp.concatenate([prod_pos, prod_neg], axis=1)
    total = lax.dot_general(
        table, both, (((0,), (0,)), ((), ())), preferred_element_type=jnp.float32
    )
    real = total[:all_slots, :half_cols] + total[:all_slots, half_cols:]
    imag = total[all_slots:, :half_cols] - total[all_slots:, half_cols:]
    scale = weight / count.astype(jnp.float32)
    joined = jnp.stack([real * scale, imag * scale], axis=-1).reshape(all_slots, columns)
    analysed_rows = [joined.astype(jnp.bfloat16)]
    analysed = jnp.stack(analysed_rows, axis=1)
    returned = lax.all_to_all(analysed, "wave", split_axis=0, concat_axis=1, tiled=True)
    returned = returned.reshape(pairs_n, 2, lat_band, columns)
    band_term = jnp.einsum(
        "pxlc,pxlk->cpk", returned, packed_leg, preferred_element_type=jnp.float32
    )
    summed = lax.psum_scatter(
        band_term.astype(jnp.bfloat16), "lev", scatter_dimension=0, tiled=True
    )
    zero_f = jnp.zeros((), jnp.float32)
    summed = summed.astype(jnp.float32)
    out_a = jnp.where(front[None], summed, zero_f)
    out_b = jnp.where(front[None], zero_f, summed)[:, :, ::-1]
    out = jnp.stack([out_a, out_b], axis=2)
    return out.reshape(summed.shape[0], slots, kmax_width)


def solution(mesh):
    return jax.shard_map(
        per_device,
        mesh=mesh,
        in_specs=(P("lev", "wave", None), P("wave", "lev", None), P(), P(), P()),
        out_specs=P("lev", "wave", None),
        check_vma=False,
    )
```

```python
import math

import jax
import jax.numpy as jnp
from jax import lax
from jax.sharding import PartitionSpec as P

TRUNC = 1279
LON_BLOCK = 768
NLONPAD = 5376


def angle_parts(count, waves, starts):
    phase = starts[:, None] % count * waves[None, :] % count
    angle = 2.0 * math.pi * phase.astype(jnp.float32) / count.astype(jnp.float32)
    return (jnp.cos(angle), jnp.sin(angle))


def compose_table(row_limit, count, waves, coarse_cos, coarse_sin, fine_cos, fine_sin, lon_rows):
    cosine = (
        coarse_cos[:, None, :] * fine_cos[None, :, :]
        - coarse_sin[:, None, :] * fine_sin[None, :, :]
    )
    sine = (
        coarse_sin[:, None, :] * fine_cos[None, :, :]
        + coarse_cos[:, None, :] * fine_sin[None, :, :]
    )
    rows_total = lon_rows.shape[0]
    cosine = cosine.reshape(rows_total, waves.shape[0])
    sine = sine.reshape(rows_total, waves.shape[0])
    usable = (lon_rows[:, None] < row_limit) & (2 * waves[None, :] < count)
    cosine = jnp.where(usable, cosine, jnp.zeros((), jnp.float32))
    sine = jnp.where(usable, -sine, jnp.zeros((), jnp.float32))
    return jnp.concatenate([cosine, sine], axis=1).astype(jnp.bfloat16)


def quadratic(grid):
    fields = grid.reshape(grid.shape[0], grid.shape[1] // 3, 3)
    vort = fields[:, :, 0]
    diverg = fields[:, :, 1]
    temper = fields[:, :, 2]
    stacked = jnp.stack([vort * temper, diverg * temper, vort * diverg], axis=-1)
    return stacked.reshape(grid.shape[0], grid.shape[1]).astype(jnp.bfloat16)


def per_device(spectral, legendre, weights, nlon, assignment):
    wave_index = lax.axis_index("wave")
    lev_index = lax.axis_index("lev")
    slots = legendre.shape[0]
    lat_band = legendre.shape[1]
    kmax_width = legendre.shape[2]
    all_slots = assignment.shape[0]
    pairs_n = slots // 2
    own_waves = lax.dynamic_slice_in_dim(assignment, wave_index * slots, slots)
    krange = lax.iota(jnp.int32, kmax_width)
    front = krange[None, :] < (kmax_width - own_waves.reshape(pairs_n, 2)[:, 0])[:, None]
    leg_pairs = legendre.reshape(pairs_n, 2, lat_band, kmax_width)
    zero_bf = jnp.zeros((), jnp.bfloat16)
    leg_a = jnp.where(front[:, None, :], leg_pairs[:, 0], zero_bf)
    leg_b = jnp.where(front[:, None, :], zero_bf, leg_pairs[:, 1, :, ::-1])
    packed_leg = jnp.stack([leg_a, leg_b], axis=1)
    spec_pairs = spectral.reshape(spectral.shape[0], pairs_n, 2, kmax_width)
    packed_spec = jnp.where(front[None], spec_pairs[:, :, 0], spec_pairs[:, :, 1, ::-1])
    spec_all = lax.all_gather(packed_spec, "lev", axis=0, tiled=True)
    columns = spec_all.shape[0]
    four_local = jnp.einsum(
        "pxlk,cpk->pxlc", packed_leg, spec_all, preferred_element_type=jnp.float32
    ).astype(jnp.bfloat16).reshape(slots, lat_band, columns)
    fourier = lax.all_to_all(four_local, "wave", split_axis=1, concat_axis=0, tiled=True)
    mine = fourier.shape[1]
    half_cols = columns // 2
    lat_index = lev_index * lat_band + wave_index * mine + 0
    count = lax.dynamic_slice_in_dim(nlon, lat_index, 1)[0]
    weight = lax.dynamic_slice_in_dim(weights, lat_index, 1)[0]
    half_rows = NLONPAD // 2
    half = count // 2
    fine_rows = lax.iota(jnp.int32, 128)
    coarse_rows = lax.iota(jnp.int32, half_rows // 128) * 128
    lon_rows = lax.iota(jnp.int32, half_rows)
    fine_cos, fine_sin = angle_parts(count, assignment, fine_rows)
    coarse_cos, coarse_sin = angle_parts(count, assignment, coarse_rows)
    table = compose_table(
        half + 1, count, assignment, coarse_cos, coarse_sin, fine_cos, fine_sin, lon_rows
    )
    pairs = fourier[:, 0, :].reshape(all_slots, half_cols, 2)
    zero_bf = jnp.zeros((), jnp.bfloat16)
    blank = jnp.zeros((all_slots, half_cols), jnp.bfloat16)
    split = jnp.concatenate(
        [
            jnp.concatenate([pairs[:, :, 0], blank], axis=1),
            jnp.concatenate([blank, pairs[:, :, 1]], axis=1),
        ],
        axis=0,
    )
    parts = jnp.dot(table, split, preferred_element_type=jnp.float32)
    even, odd = parts[:, :half_cols], parts[:, half_cols:]
    grid_pos = 2.0 * (even + odd)
    grid_neg = 2.0 * (even - odd)
    mirrored = (lon_rows > 0) & (lon_rows < half)
    prod_pos = quadratic(grid_pos)
    prod_neg = jnp.where(mirrored[:, None], quadratic(grid_neg), zero_bf)
    both = jnp.concatenate([prod_pos, prod_neg], axis=1)
    total = lax.dot_general(
        table, both, (((0,), (0,)), ((), ())), preferred_element_type=jnp.float32
    )
    real = total[:all_slots, :half_cols] + total[:all_slots, half_cols:]
    imag = total[all_slots:, :half_cols] - total[all_slots:, half_cols:]
    scale = weight / count.astype(jnp.float32)
    joined = jnp.stack([real * scale, imag * scale], axis=-1).reshape(all_slots, columns)
    analysed_rows = [joined.astype(jnp.bfloat16)]
    analysed = jnp.stack(analysed_rows, axis=1)
    returned = lax.all_to_all(analysed, "wave", split_axis=0, concat_axis=1, tiled=True)
    returned = returned.reshape(pairs_n, 2, lat_band, columns)
    band_term = jnp.einsum(
        "pxlc,pxlk->cpk", returned, packed_leg, preferred_element_type=jnp.float32
    )
    lev_count = lax.axis_size("lev")
    shares = band_term.astype(jnp.bfloat16).reshape(
        lev_count, columns // lev_count, pairs_n, kmax_width
    )
    gathered = lax.all_to_all(shares, "lev", split_axis=0, concat_axis=0, tiled=True)
    summed = jnp.sum(gathered.astype(jnp.float32), axis=0)
    zero_f = jnp.zeros((), jnp.float32)
    out_a = jnp.where(front[None], summed, zero_f)
    out_b = jnp.where(front[None], zero_f, summed)[:, :, ::-1]
    out = jnp.stack([out_a, out_b], axis=2)
    return out.reshape(summed.shape[0], slots, kmax_width)


def solution(mesh):
    return jax.shard_map(
        per_device,
        mesh=mesh,
        in_specs=(P("lev", "wave", None), P("wave", "lev", None), P(), P(), P()),
        out_specs=P("lev", "wave", None),
        check_vma=False,
    )
```

```python
import math

import jax
import jax.numpy as jnp
from jax import lax
from jax.sharding import PartitionSpec as P

TRUNC = 1279
LON_BLOCK = 768
NLONPAD = 5376
LEV = ("chip", "core")


def angle_parts(count, waves, starts):
    phase = starts[:, None] % count * waves[None, :] % count
    angle = 2.0 * math.pi * phase.astype(jnp.float32) / count.astype(jnp.float32)
    return (jnp.cos(angle), jnp.sin(angle))


def compose_table(row_limit, count, waves, coarse_cos, coarse_sin, fine_cos, fine_sin, lon_rows):
    cosine = (
        coarse_cos[:, None, :] * fine_cos[None, :, :]
        - coarse_sin[:, None, :] * fine_sin[None, :, :]
    )
    sine = (
        coarse_sin[:, None, :] * fine_cos[None, :, :]
        + coarse_cos[:, None, :] * fine_sin[None, :, :]
    )
    rows_total = lon_rows.shape[0]
    cosine = cosine.reshape(rows_total, waves.shape[0])
    sine = sine.reshape(rows_total, waves.shape[0])
    usable = (lon_rows[:, None] < row_limit) & (2 * waves[None, :] < count)
    cosine = jnp.where(usable, cosine, jnp.zeros((), jnp.float32))
    sine = jnp.where(usable, -sine, jnp.zeros((), jnp.float32))
    return jnp.concatenate([cosine, sine], axis=1).astype(jnp.bfloat16)


def quadratic(grid):
    fields = grid.reshape(grid.shape[0], grid.shape[1] // 3, 3)
    vort = fields[:, :, 0]
    diverg = fields[:, :, 1]
    temper = fields[:, :, 2]
    stacked = jnp.stack([vort * temper, diverg * temper, vort * diverg], axis=-1)
    return stacked.reshape(grid.shape[0], grid.shape[1]).astype(jnp.bfloat16)


def per_device(spectral, legendre, weights, nlon, assignment):
    wave_index = lax.axis_index("wave")
    lev_index = lax.axis_index("chip") * lax.axis_size("core") + lax.axis_index("core")
    slots = legendre.shape[0]
    lat_band = legendre.shape[1]
    kmax_width = legendre.shape[2]
    all_slots = assignment.shape[0]
    pairs_n = slots // 2
    own_waves = lax.dynamic_slice_in_dim(assignment, wave_index * slots, slots)
    krange = lax.iota(jnp.int32, kmax_width)
    front = krange[None, :] < (kmax_width - own_waves.reshape(pairs_n, 2)[:, 0])[:, None]
    leg_pairs = legendre.reshape(pairs_n, 2, lat_band, kmax_width)
    zero_bf = jnp.zeros((), jnp.bfloat16)
    leg_a = jnp.where(front[:, None, :], leg_pairs[:, 0], zero_bf)
    leg_b = jnp.where(front[:, None, :], zero_bf, leg_pairs[:, 1, :, ::-1])
    packed_leg = jnp.stack([leg_a, leg_b], axis=1)
    spec_pairs = spectral.reshape(spectral.shape[0], pairs_n, 2, kmax_width)
    packed_spec = jnp.where(front[None], spec_pairs[:, :, 0], spec_pairs[:, :, 1, ::-1])
    spec_all = lax.all_gather(packed_spec, LEV, axis=0, tiled=True)
    columns = spec_all.shape[0]
    four_local = jnp.einsum(
        "pxlk,cpk->pxlc", packed_leg, spec_all, preferred_element_type=jnp.float32
    ).astype(jnp.bfloat16).reshape(slots, lat_band, columns)
    fourier = lax.all_to_all(four_local, "wave", split_axis=1, concat_axis=0, tiled=True)
    mine = fourier.shape[1]
    half_cols = columns // 2
    lat_index = lev_index * lat_band + wave_index * mine + 0
    count = lax.dynamic_slice_in_dim(nlon, lat_index, 1)[0]
    weight = lax.dynamic_slice_in_dim(weights, lat_index, 1)[0]
    half_rows = NLONPAD // 2
    half = count // 2
    fine_rows = lax.iota(jnp.int32, 128)
    coarse_rows = lax.iota(jnp.int32, half_rows // 128) * 128
    lon_rows = lax.iota(jnp.int32, half_rows)
    fine_cos, fine_sin = angle_parts(count, assignment, fine_rows)
    coarse_cos, coarse_sin = angle_parts(count, assignment, coarse_rows)
    table = compose_table(
        half + 1, count, assignment, coarse_cos, coarse_sin, fine_cos, fine_sin, lon_rows
    )
    pairs = fourier[:, 0, :].reshape(all_slots, half_cols, 2)
    zero_bf = jnp.zeros((), jnp.bfloat16)
    blank = jnp.zeros((all_slots, half_cols), jnp.bfloat16)
    split = jnp.concatenate(
        [
            jnp.concatenate([pairs[:, :, 0], blank], axis=1),
            jnp.concatenate([blank, pairs[:, :, 1]], axis=1),
        ],
        axis=0,
    )
    parts = jnp.dot(table, split, preferred_element_type=jnp.float32)
    even, odd = parts[:, :half_cols], parts[:, half_cols:]
    grid_pos = 2.0 * (even + odd)
    grid_neg = 2.0 * (even - odd)
    mirrored = (lon_rows > 0) & (lon_rows < half)
    prod_pos = quadratic(grid_pos)
    prod_neg = jnp.where(mirrored[:, None], quadratic(grid_neg), zero_bf)
    both = jnp.concatenate([prod_pos, prod_neg], axis=1)
    total = lax.dot_general(
        table, both, (((0,), (0,)), ((), ())), preferred_element_type=jnp.float32
    )
    real = total[:all_slots, :half_cols] + total[:all_slots, half_cols:]
    imag = total[all_slots:, :half_cols] - total[all_slots:, half_cols:]
    scale = weight / count.astype(jnp.float32)
    joined = jnp.stack([real * scale, imag * scale], axis=-1).reshape(all_slots, columns)
    analysed_rows = [joined.astype(jnp.bfloat16)]
    analysed = jnp.stack(analysed_rows, axis=1)
    returned = lax.all_to_all(analysed, "wave", split_axis=0, concat_axis=1, tiled=True)
    returned = returned.reshape(pairs_n, 2, lat_band, columns)
    band_term = jnp.einsum(
        "pxlc,pxlk->cpk", returned, packed_leg, preferred_element_type=jnp.float32
    )
    chips = lax.axis_size("chip")
    cores = lax.axis_size("core")
    core_index = lax.axis_index("core")
    shares = band_term.astype(jnp.bfloat16).reshape(
        chips, cores, columns // (chips * cores), pairs_n, kmax_width
    )
    keep = lax.dynamic_index_in_dim(shares, core_index, axis=1, keepdims=False)
    give = lax.dynamic_index_in_dim(shares, cores - 1 - core_index, axis=1, keepdims=False)
    got = lax.ppermute(give, "core", [(0, 1), (1, 0)])
    pair_sum = (keep.astype(jnp.float32) + got.astype(jnp.float32)).astype(jnp.bfloat16)
    gathered = lax.all_to_all(pair_sum, "chip", split_axis=0, concat_axis=0, tiled=True)
    summed = jnp.sum(gathered.astype(jnp.float32), axis=0)
    zero_f = jnp.zeros((), jnp.float32)
    out_a = jnp.where(front[None], summed, zero_f)
    out_b = jnp.where(front[None], zero_f, summed)[:, :, ::-1]
    out = jnp.stack([out_a, out_b], axis=2)
    return out.reshape(summed.shape[0], slots, kmax_width)


def solution(mesh):
    grid = mesh.devices.reshape(mesh.shape["wave"], mesh.shape["lev"] // 2, 2)
    split_mesh = jax.sharding.Mesh(grid, ("wave", "chip", "core"))
    return jax.shard_map(
        per_device,
        mesh=split_mesh,
        in_specs=(P(LEV, "wave", None), P("wave", LEV, None), P(), P(), P()),
        out_specs=P(LEV, "wave", None),
        check_vma=False,
    )
```

```python
import math

import jax
import jax.numpy as jnp
from jax import lax
from jax.sharding import PartitionSpec as P

TRUNC = 1279
LON_BLOCK = 768
NLONPAD = 5376
LEV = ("chip", "core")


def angle_parts(count, waves, starts):
    phase = starts[:, None] % count * waves[None, :] % count
    angle = 2.0 * math.pi * phase.astype(jnp.float32) / count.astype(jnp.float32)
    return (jnp.cos(angle), jnp.sin(angle))


def compose_table(row_limit, count, waves, coarse_cos, coarse_sin, fine_cos, fine_sin, lon_rows):
    cosine = (
        coarse_cos[:, None, :] * fine_cos[None, :, :]
        - coarse_sin[:, None, :] * fine_sin[None, :, :]
    )
    sine = (
        coarse_sin[:, None, :] * fine_cos[None, :, :]
        + coarse_cos[:, None, :] * fine_sin[None, :, :]
    )
    rows_total = lon_rows.shape[0]
    cosine = cosine.reshape(rows_total, waves.shape[0])
    sine = sine.reshape(rows_total, waves.shape[0])
    usable = (lon_rows[:, None] < row_limit) & (2 * waves[None, :] < count)
    cosine = jnp.where(usable, cosine, jnp.zeros((), jnp.float32))
    sine = jnp.where(usable, -sine, jnp.zeros((), jnp.float32))
    return jnp.concatenate([cosine, sine], axis=1).astype(jnp.bfloat16)


def quadratic(grid):
    fields = grid.reshape(grid.shape[0], grid.shape[1] // 3, 3)
    vort = fields[:, :, 0]
    diverg = fields[:, :, 1]
    temper = fields[:, :, 2]
    stacked = jnp.stack([vort * temper, diverg * temper, vort * diverg], axis=-1)
    return stacked.reshape(grid.shape[0], grid.shape[1]).astype(jnp.bfloat16)


def ring_reduce(shares, axis):
    size = lax.axis_size(axis)
    me = lax.axis_index(axis)
    half = shares.shape[-1] // 2
    lanes = (shares[..., :half], shares[..., half:])
    steps = ((1, [(i, (i + 1) % size) for i in range(size)]),
             (-1, [(i, (i - 1) % size) for i in range(size)]))
    ends = []
    for lane, (sign, perm) in zip(lanes, steps):
        acc = lax.dynamic_index_in_dim(lane, (me - sign) % size, axis=0, keepdims=False)
        acc = acc.astype(jnp.float32)
        for step in range(size - 1):
            moved = lax.ppermute(acc.astype(jnp.bfloat16), axis, perm)
            mine = lax.dynamic_index_in_dim(
                lane, (me - sign * (step + 2)) % size, axis=0, keepdims=False
            )
            acc = moved.astype(jnp.float32) + mine.astype(jnp.float32)
        ends.append(acc)
    return jnp.concatenate(ends, axis=-1)


def per_device(spectral, legendre, weights, nlon, assignment):
    wave_index = lax.axis_index("wave")
    lev_index = lax.axis_index("chip") * lax.axis_size("core") + lax.axis_index("core")
    slots = legendre.shape[0]
    lat_band = legendre.shape[1]
    kmax_width = legendre.shape[2]
    all_slots = assignment.shape[0]
    pairs_n = slots // 2
    own_waves = lax.dynamic_slice_in_dim(assignment, wave_index * slots, slots)
    krange = lax.iota(jnp.int32, kmax_width)
    front = krange[None, :] < (kmax_width - own_waves.reshape(pairs_n, 2)[:, 0])[:, None]
    leg_pairs = legendre.reshape(pairs_n, 2, lat_band, kmax_width)
    zero_bf = jnp.zeros((), jnp.bfloat16)
    leg_a = jnp.where(front[:, None, :], leg_pairs[:, 0], zero_bf)
    leg_b = jnp.where(front[:, None, :], zero_bf, leg_pairs[:, 1, :, ::-1])
    packed_leg = jnp.stack([leg_a, leg_b], axis=1)
    spec_pairs = spectral.reshape(spectral.shape[0], pairs_n, 2, kmax_width)
    packed_spec = jnp.where(front[None], spec_pairs[:, :, 0], spec_pairs[:, :, 1, ::-1])
    spec_all = lax.all_gather(packed_spec, LEV, axis=0, tiled=True)
    columns = spec_all.shape[0]
    four_local = jnp.einsum(
        "pxlk,cpk->pxlc", packed_leg, spec_all, preferred_element_type=jnp.float32
    ).astype(jnp.bfloat16).reshape(slots, lat_band, columns)
    fourier = lax.all_to_all(four_local, "wave", split_axis=1, concat_axis=0, tiled=True)
    mine = fourier.shape[1]
    half_cols = columns // 2
    lat_index = lev_index * lat_band + wave_index * mine + 0
    count = lax.dynamic_slice_in_dim(nlon, lat_index, 1)[0]
    weight = lax.dynamic_slice_in_dim(weights, lat_index, 1)[0]
    half_rows = NLONPAD // 2
    half = count // 2
    fine_rows = lax.iota(jnp.int32, 128)
    coarse_rows = lax.iota(jnp.int32, half_rows // 128) * 128
    lon_rows = lax.iota(jnp.int32, half_rows)
    fine_cos, fine_sin = angle_parts(count, assignment, fine_rows)
    coarse_cos, coarse_sin = angle_parts(count, assignment, coarse_rows)
    table = compose_table(
        half + 1, count, assignment, coarse_cos, coarse_sin, fine_cos, fine_sin, lon_rows
    )
    pairs = fourier[:, 0, :].reshape(all_slots, half_cols, 2)
    zero_bf = jnp.zeros((), jnp.bfloat16)
    blank = jnp.zeros((all_slots, half_cols), jnp.bfloat16)
    split = jnp.concatenate(
        [
            jnp.concatenate([pairs[:, :, 0], blank], axis=1),
            jnp.concatenate([blank, pairs[:, :, 1]], axis=1),
        ],
        axis=0,
    )
    parts = jnp.dot(table, split, preferred_element_type=jnp.float32)
    even, odd = parts[:, :half_cols], parts[:, half_cols:]
    grid_pos = 2.0 * (even + odd)
    grid_neg = 2.0 * (even - odd)
    mirrored = (lon_rows > 0) & (lon_rows < half)
    prod_pos = quadratic(grid_pos)
    prod_neg = jnp.where(mirrored[:, None], quadratic(grid_neg), zero_bf)
    both = jnp.concatenate([prod_pos, prod_neg], axis=1)
    total = lax.dot_general(
        table, both, (((0,), (0,)), ((), ())), preferred_element_type=jnp.float32
    )
    real = total[:all_slots, :half_cols] + total[:all_slots, half_cols:]
    imag = total[all_slots:, :half_cols] - total[all_slots:, half_cols:]
    scale = weight / count.astype(jnp.float32)
    joined = jnp.stack([real * scale, imag * scale], axis=-1).reshape(all_slots, columns)
    analysed_rows = [joined.astype(jnp.bfloat16)]
    analysed = jnp.stack(analysed_rows, axis=1)
    returned = lax.all_to_all(analysed, "wave", split_axis=0, concat_axis=1, tiled=True)
    returned = returned.reshape(pairs_n, 2, lat_band, columns)
    band_term = jnp.einsum(
        "pxlc,pxlk->cpk", returned, packed_leg, preferred_element_type=jnp.float32
    )
    chips = lax.axis_size("chip")
    cores = lax.axis_size("core")
    core_index = lax.axis_index("core")
    shares = band_term.astype(jnp.bfloat16).reshape(
        chips, cores, columns // (chips * cores), pairs_n, kmax_width
    )
    keep = lax.dynamic_index_in_dim(shares, core_index, axis=1, keepdims=False)
    give = lax.dynamic_index_in_dim(shares, cores - 1 - core_index, axis=1, keepdims=False)
    got = lax.ppermute(give, "core", [(0, 1), (1, 0)])
    pair_sum = (keep.astype(jnp.float32) + got.astype(jnp.float32)).astype(jnp.bfloat16)
    summed = ring_reduce(pair_sum, "chip")
    zero_f = jnp.zeros((), jnp.float32)
    out_a = jnp.where(front[None], summed, zero_f)
    out_b = jnp.where(front[None], zero_f, summed)[:, :, ::-1]
    out = jnp.stack([out_a, out_b], axis=2)
    return out.reshape(summed.shape[0], slots, kmax_width)


def solution(mesh):
    grid = mesh.devices.reshape(mesh.shape["wave"], mesh.shape["lev"] // 2, 2)
    split_mesh = jax.sharding.Mesh(grid, ("wave", "chip", "core"))
    return jax.shard_map(
        per_device,
        mesh=split_mesh,
        in_specs=(P(LEV, "wave", None), P("wave", LEV, None), P(), P(), P()),
        out_specs=P(LEV, "wave", None),
        check_vma=False,
    )
```

```python
import math

import jax
import jax.numpy as jnp
from jax import lax
from jax.sharding import PartitionSpec as P

TRUNC = 1279
LON_BLOCK = 768
NLONPAD = 5376
LEV = ("chip", "core")


def angle_parts(count, waves, starts):
    phase = starts[:, None] % count * waves[None, :] % count
    angle = 2.0 * math.pi * phase.astype(jnp.float32) / count.astype(jnp.float32)
    return (jnp.cos(angle), jnp.sin(angle))


def compose_table(row_limit, count, waves, coarse_cos, coarse_sin, fine_cos, fine_sin, lon_rows):
    cosine = (
        coarse_cos[:, None, :] * fine_cos[None, :, :]
        - coarse_sin[:, None, :] * fine_sin[None, :, :]
    )
    sine = (
        coarse_sin[:, None, :] * fine_cos[None, :, :]
        + coarse_cos[:, None, :] * fine_sin[None, :, :]
    )
    rows_total = lon_rows.shape[0]
    cosine = cosine.reshape(rows_total, waves.shape[0])
    sine = sine.reshape(rows_total, waves.shape[0])
    usable = (lon_rows[:, None] < row_limit) & (2 * waves[None, :] < count)
    cosine = jnp.where(usable, cosine, jnp.zeros((), jnp.float32))
    sine = jnp.where(usable, -sine, jnp.zeros((), jnp.float32))
    return jnp.concatenate([cosine, sine], axis=1).astype(jnp.bfloat16)


def quadratic(grid):
    fields = grid.reshape(grid.shape[0], grid.shape[1] // 3, 3)
    vort = fields[:, :, 0]
    diverg = fields[:, :, 1]
    temper = fields[:, :, 2]
    stacked = jnp.stack([vort * temper, diverg * temper, vort * diverg], axis=-1)
    return stacked.reshape(grid.shape[0], grid.shape[1]).astype(jnp.bfloat16)


def core_swap(block):
    other = lax.ppermute(block, "core", [(0, 1), (1, 0)])
    first = lax.axis_index("core") == 0
    return jnp.where(first, block, other), jnp.where(first, other, block)


def chip_gather(block):
    chips = lax.axis_size("chip")
    core_index = lax.axis_index("core")
    low, high = core_swap(block)
    pair_block = jnp.concatenate([low, high], axis=0)
    share = block.shape[1] // 2
    half = lax.dynamic_slice_in_dim(pair_block, core_index * share, share, axis=1)
    sent = jnp.broadcast_to(half[None], (chips,) + half.shape)
    got = lax.all_to_all(sent, "chip", split_axis=0, concat_axis=0, tiled=True)
    got = got.reshape((chips * half.shape[0],) + half.shape[1:])
    low, high = core_swap(got)
    return jnp.concatenate([low, high], axis=1)


def per_device(spectral, legendre, weights, nlon, assignment):
    wave_index = lax.axis_index("wave")
    lev_index = lax.axis_index("chip") * lax.axis_size("core") + lax.axis_index("core")
    slots = legendre.shape[0]
    lat_band = legendre.shape[1]
    kmax_width = legendre.shape[2]
    all_slots = assignment.shape[0]
    pairs_n = slots // 2
    own_waves = lax.dynamic_slice_in_dim(assignment, wave_index * slots, slots)
    krange = lax.iota(jnp.int32, kmax_width)
    front = krange[None, :] < (kmax_width - own_waves.reshape(pairs_n, 2)[:, 0])[:, None]
    leg_pairs = legendre.reshape(pairs_n, 2, lat_band, kmax_width)
    zero_bf = jnp.zeros((), jnp.bfloat16)
    leg_a = jnp.where(front[:, None, :], leg_pairs[:, 0], zero_bf)
    leg_b = jnp.where(front[:, None, :], zero_bf, leg_pairs[:, 1, :, ::-1])
    packed_leg = jnp.stack([leg_a, leg_b], axis=1)
    spec_pairs = spectral.reshape(spectral.shape[0], pairs_n, 2, kmax_width)
    packed_spec = jnp.where(front[None], spec_pairs[:, :, 0], spec_pairs[:, :, 1, ::-1])
    spec_all = chip_gather(packed_spec)
    columns = spec_all.shape[0]
    four_local = jnp.einsum(
        "pxlk,cpk->pxlc", packed_leg, spec_all, preferred_element_type=jnp.float32
    ).astype(jnp.bfloat16).reshape(slots, lat_band, columns)
    fourier = lax.all_to_all(four_local, "wave", split_axis=1, concat_axis=0, tiled=True)
    mine = fourier.shape[1]
    half_cols = columns // 2
    lat_index = lev_index * lat_band + wave_index * mine + 0
    count = lax.dynamic_slice_in_dim(nlon, lat_index, 1)[0]
    weight = lax.dynamic_slice_in_dim(weights, lat_index, 1)[0]
    half_rows = NLONPAD // 2
    half = count // 2
    fine_rows = lax.iota(jnp.int32, 128)
    coarse_rows = lax.iota(jnp.int32, half_rows // 128) * 128
    lon_rows = lax.iota(jnp.int32, half_rows)
    fine_cos, fine_sin = angle_parts(count, assignment, fine_rows)
    coarse_cos, coarse_sin = angle_parts(count, assignment, coarse_rows)
    table = compose_table(
        half + 1, count, assignment, coarse_cos, coarse_sin, fine_cos, fine_sin, lon_rows
    )
    pairs = fourier[:, 0, :].reshape(all_slots, half_cols, 2)
    zero_bf = jnp.zeros((), jnp.bfloat16)
    blank = jnp.zeros((all_slots, half_cols), jnp.bfloat16)
    split = jnp.concatenate(
        [
            jnp.concatenate([pairs[:, :, 0], blank], axis=1),
            jnp.concatenate([blank, pairs[:, :, 1]], axis=1),
        ],
        axis=0,
    )
    parts = jnp.dot(table, split, preferred_element_type=jnp.float32)
    even, odd = parts[:, :half_cols], parts[:, half_cols:]
    grid_pos = 2.0 * (even + odd)
    grid_neg = 2.0 * (even - odd)
    mirrored = (lon_rows > 0) & (lon_rows < half)
    prod_pos = quadratic(grid_pos)
    prod_neg = jnp.where(mirrored[:, None], quadratic(grid_neg), zero_bf)
    both = jnp.concatenate([prod_pos, prod_neg], axis=1)
    total = lax.dot_general(
        table, both, (((0,), (0,)), ((), ())), preferred_element_type=jnp.float32
    )
    real = total[:all_slots, :half_cols] + total[:all_slots, half_cols:]
    imag = total[all_slots:, :half_cols] - total[all_slots:, half_cols:]
    scale = weight / count.astype(jnp.float32)
    joined = jnp.stack([real * scale, imag * scale], axis=-1).reshape(all_slots, columns)
    analysed_rows = [joined.astype(jnp.bfloat16)]
    analysed = jnp.stack(analysed_rows, axis=1)
    returned = lax.all_to_all(analysed, "wave", split_axis=0, concat_axis=1, tiled=True)
    returned = returned.reshape(pairs_n, 2, lat_band, columns)
    band_term = jnp.einsum(
        "pxlc,pxlk->cpk", returned, packed_leg, preferred_element_type=jnp.float32
    )
    chips = lax.axis_size("chip")
    cores = lax.axis_size("core")
    core_index = lax.axis_index("core")
    shares = band_term.astype(jnp.bfloat16).reshape(
        chips, cores, columns // (chips * cores), pairs_n, kmax_width
    )
    keep = lax.dynamic_index_in_dim(shares, core_index, axis=1, keepdims=False)
    give = lax.dynamic_index_in_dim(shares, cores - 1 - core_index, axis=1, keepdims=False)
    got = lax.ppermute(give, "core", [(0, 1), (1, 0)])
    pair_sum = (keep.astype(jnp.float32) + got.astype(jnp.float32)).astype(jnp.bfloat16)
    gathered = lax.all_to_all(pair_sum, "chip", split_axis=0, concat_axis=0, tiled=True)
    summed = jnp.sum(gathered.astype(jnp.float32), axis=0)
    zero_f = jnp.zeros((), jnp.float32)
    out_a = jnp.where(front[None], summed, zero_f)
    out_b = jnp.where(front[None], zero_f, summed)[:, :, ::-1]
    out = jnp.stack([out_a, out_b], axis=2)
    return out.reshape(summed.shape[0], slots, kmax_width)


def solution(mesh):
    grid = mesh.devices.reshape(mesh.shape["wave"], mesh.shape["lev"] // 2, 2)
    split_mesh = jax.sharding.Mesh(grid, ("wave", "chip", "core"))
    return jax.shard_map(
        per_device,
        mesh=split_mesh,
        in_specs=(P(LEV, "wave", None), P("wave", LEV, None), P(), P(), P()),
        out_specs=P(LEV, "wave", None),
        check_vma=False,
    )
```

```python
import math

import jax
import jax.numpy as jnp
from jax import lax
from jax.sharding import PartitionSpec as P

TRUNC = 1279
LON_BLOCK = 768
NLONPAD = 5376
LEV = ("chip", "core")


def angle_parts(count, waves, starts):
    phase = starts[:, None] % count * waves[None, :] % count
    angle = 2.0 * math.pi * phase.astype(jnp.float32) / count.astype(jnp.float32)
    return (jnp.cos(angle), jnp.sin(angle))


def compose_table(row_limit, count, waves, coarse_cos, coarse_sin, fine_cos, fine_sin, lon_rows):
    cosine = (
        coarse_cos[:, None, :] * fine_cos[None, :, :]
        - coarse_sin[:, None, :] * fine_sin[None, :, :]
    )
    sine = (
        coarse_sin[:, None, :] * fine_cos[None, :, :]
        + coarse_cos[:, None, :] * fine_sin[None, :, :]
    )
    rows_total = lon_rows.shape[0]
    cosine = cosine.reshape(rows_total, waves.shape[0])
    sine = sine.reshape(rows_total, waves.shape[0])
    usable = (lon_rows[:, None] < row_limit) & (2 * waves[None, :] < count)
    cosine = jnp.where(usable, cosine, jnp.zeros((), jnp.float32))
    sine = jnp.where(usable, -sine, jnp.zeros((), jnp.float32))
    return jnp.concatenate([cosine, sine], axis=1).astype(jnp.bfloat16)


def quadratic(grid):
    fields = grid.reshape(grid.shape[0], grid.shape[1] // 3, 3)
    vort = fields[:, :, 0]
    diverg = fields[:, :, 1]
    temper = fields[:, :, 2]
    stacked = jnp.stack([vort * temper, diverg * temper, vort * diverg], axis=-1)
    return stacked.reshape(grid.shape[0], grid.shape[1]).astype(jnp.bfloat16)


def core_swap(block):
    other = lax.ppermute(block, "core", [(0, 1), (1, 0)])
    first = lax.axis_index("core") == 0
    return jnp.where(first, block, other), jnp.where(first, other, block)


def chip_gather(block):
    chips = lax.axis_size("chip")
    core_index = lax.axis_index("core")
    low, high = core_swap(block)
    pair_block = jnp.concatenate([low, high], axis=0)
    share = block.shape[1] // 2
    half = lax.dynamic_slice_in_dim(pair_block, core_index * share, share, axis=1)
    sent = jnp.broadcast_to(half[None], (chips,) + half.shape)
    got = lax.all_to_all(sent, "chip", split_axis=0, concat_axis=0, tiled=True)
    got = got.reshape((chips * half.shape[0],) + half.shape[1:])
    low, high = core_swap(got)
    return jnp.concatenate([low, high], axis=1)


def per_device(spectral, legendre, weights, nlon, assignment):
    wave_index = lax.axis_index("wave")
    lev_index = lax.axis_index("chip") * lax.axis_size("core") + lax.axis_index("core")
    slots = legendre.shape[0]
    lat_band = legendre.shape[1]
    kmax_width = legendre.shape[2]
    all_slots = assignment.shape[0]
    pairs_n = slots // 2
    own_waves = lax.dynamic_slice_in_dim(assignment, wave_index * slots, slots)
    krange = lax.iota(jnp.int32, kmax_width)
    front = krange[None, :] < (kmax_width - own_waves.reshape(pairs_n, 2)[:, 0])[:, None]
    leg_pairs = legendre.reshape(pairs_n, 2, lat_band, kmax_width)
    zero_bf = jnp.zeros((), jnp.bfloat16)
    leg_a = jnp.where(front[:, None, :], leg_pairs[:, 0], zero_bf)
    leg_b = jnp.where(front[:, None, :], zero_bf, leg_pairs[:, 1, :, ::-1])
    packed_leg = jnp.stack([leg_a, leg_b], axis=1)
    spec_pairs = spectral.reshape(spectral.shape[0], pairs_n, 2, kmax_width)
    packed_spec = jnp.where(front[None], spec_pairs[:, :, 0], spec_pairs[:, :, 1, ::-1])
    spec_all = chip_gather(packed_spec)
    columns = spec_all.shape[0]
    four_local = jnp.einsum(
        "pxlk,cpk->pxlc", packed_leg, spec_all, preferred_element_type=jnp.float32
    ).astype(jnp.bfloat16).reshape(slots, lat_band, columns)
    fourier = lax.all_to_all(four_local, "wave", split_axis=1, concat_axis=0, tiled=True)
    mine = fourier.shape[1]
    half_cols = columns // 2
    lat_index = lev_index * lat_band + wave_index * mine + 0
    count = lax.dynamic_slice_in_dim(nlon, lat_index, 1)[0]
    weight = lax.dynamic_slice_in_dim(weights, lat_index, 1)[0]
    half_rows = NLONPAD // 2
    half = count // 2
    fine_rows = lax.iota(jnp.int32, 128)
    coarse_rows = lax.iota(jnp.int32, half_rows // 128) * 128
    lon_rows = lax.iota(jnp.int32, half_rows)
    fine_cos, fine_sin = angle_parts(count, assignment, fine_rows)
    coarse_cos, coarse_sin = angle_parts(count, assignment, coarse_rows)
    table = compose_table(
        half + 1, count, assignment, coarse_cos, coarse_sin, fine_cos, fine_sin, lon_rows
    )
    pairs = fourier[:, 0, :].reshape(all_slots, half_cols, 2)
    zero_bf = jnp.zeros((), jnp.bfloat16)
    blank = jnp.zeros((all_slots, half_cols), jnp.bfloat16)
    split = jnp.concatenate(
        [
            jnp.concatenate([pairs[:, :, 0], blank], axis=1),
            jnp.concatenate([blank, pairs[:, :, 1]], axis=1),
        ],
        axis=0,
    )
    parts = jnp.dot(table, split, preferred_element_type=jnp.float32)
    even, odd = parts[:, :half_cols], parts[:, half_cols:]
    grid_pos = 2.0 * (even + odd)
    grid_neg = 2.0 * (even - odd)
    mirrored = (lon_rows > 0) & (lon_rows < half)
    prod_pos = quadratic(grid_pos)
    prod_neg = jnp.where(mirrored[:, None], quadratic(grid_neg), zero_bf)
    both = jnp.concatenate([prod_pos, prod_neg], axis=1)
    total = lax.dot_general(
        table, both, (((0,), (0,)), ((), ())), preferred_element_type=jnp.float32
    )
    real = total[:all_slots, :half_cols] + total[:all_slots, half_cols:]
    imag = total[all_slots:, :half_cols] - total[all_slots:, half_cols:]
    scale = weight / count.astype(jnp.float32)
    joined = jnp.stack([real * scale, imag * scale], axis=-1).reshape(all_slots, columns)
    analysed_rows = [joined.astype(jnp.bfloat16)]
    analysed = jnp.stack(analysed_rows, axis=1)
    returned = lax.all_to_all(analysed, "wave", split_axis=0, concat_axis=1, tiled=True)
    returned = returned.reshape(pairs_n, 2, lat_band, columns)
    band_term = jnp.einsum(
        "pxlc,pxlk->cpk", returned, packed_leg, preferred_element_type=jnp.float32
    )
    chips = lax.axis_size("chip")
    cores = lax.axis_size("core")
    core_index = lax.axis_index("core")
    shares = band_term.astype(jnp.bfloat16).reshape(
        chips, cores, columns // (chips * cores), pairs_n, kmax_width
    )
    keep = lax.dynamic_index_in_dim(shares, core_index, axis=1, keepdims=False)
    give = lax.dynamic_index_in_dim(shares, cores - 1 - core_index, axis=1, keepdims=False)
    sums = []
    step = pairs_n // 2
    for start in (0, step):
        got = lax.ppermute(give[:, :, start:start + step], "core", [(0, 1), (1, 0)])
        pair_sum = (
            keep[:, :, start:start + step].astype(jnp.float32) + got.astype(jnp.float32)
        ).astype(jnp.bfloat16)
        gathered = lax.all_to_all(pair_sum, "chip", split_axis=0, concat_axis=0, tiled=True)
        sums.append(jnp.sum(gathered.astype(jnp.float32), axis=0))
    summed = jnp.concatenate(sums, axis=1)
    zero_f = jnp.zeros((), jnp.float32)
    out_a = jnp.where(front[None], summed, zero_f)
    out_b = jnp.where(front[None], zero_f, summed)[:, :, ::-1]
    out = jnp.stack([out_a, out_b], axis=2)
    return out.reshape(summed.shape[0], slots, kmax_width)


def solution(mesh):
    grid = mesh.devices.reshape(mesh.shape["wave"], mesh.shape["lev"] // 2, 2)
    split_mesh = jax.sharding.Mesh(grid, ("wave", "chip", "core"))
    return jax.shard_map(
        per_device,
        mesh=split_mesh,
        in_specs=(P(LEV, "wave", None), P("wave", LEV, None), P(), P(), P()),
        out_specs=P(LEV, "wave", None),
        check_vma=False,
    )
```

```python
import math

import jax
import jax.numpy as jnp
from jax import lax
from jax.sharding import PartitionSpec as P

TRUNC = 1279
LON_BLOCK = 768
NLONPAD = 5376
LEV = ("chip", "core")


def angle_parts(count, waves, starts):
    phase = starts[:, None] % count * waves[None, :] % count
    angle = 2.0 * math.pi * phase.astype(jnp.float32) / count.astype(jnp.float32)
    return (jnp.cos(angle), jnp.sin(angle))


def compose_table(row_limit, count, waves, coarse_cos, coarse_sin, fine_cos, fine_sin, lon_rows):
    cosine = (
        coarse_cos[:, None, :] * fine_cos[None, :, :]
        - coarse_sin[:, None, :] * fine_sin[None, :, :]
    )
    sine = (
        coarse_sin[:, None, :] * fine_cos[None, :, :]
        + coarse_cos[:, None, :] * fine_sin[None, :, :]
    )
    rows_total = lon_rows.shape[0]
    cosine = cosine.reshape(rows_total, waves.shape[0])
    sine = sine.reshape(rows_total, waves.shape[0])
    usable = (lon_rows[:, None] < row_limit) & (2 * waves[None, :] < count)
    cosine = jnp.where(usable, cosine, jnp.zeros((), jnp.float32))
    sine = jnp.where(usable, -sine, jnp.zeros((), jnp.float32))
    return jnp.concatenate([cosine, sine], axis=1).astype(jnp.bfloat16)


def quadratic(grid):
    fields = grid.reshape(grid.shape[0], grid.shape[1] // 3, 3)
    vort = fields[:, :, 0]
    diverg = fields[:, :, 1]
    temper = fields[:, :, 2]
    stacked = jnp.stack([vort * temper, diverg * temper, vort * diverg], axis=-1)
    return stacked.reshape(grid.shape[0], grid.shape[1]).astype(jnp.bfloat16)


def core_swap(block):
    other = lax.ppermute(block, "core", [(0, 1), (1, 0)])
    first = lax.axis_index("core") == 0
    return jnp.where(first, block, other), jnp.where(first, other, block)


def chip_gather(block):
    chips = lax.axis_size("chip")
    core_index = lax.axis_index("core")
    low, high = core_swap(block)
    pair_block = jnp.concatenate([low, high], axis=0)
    share = block.shape[1] // 2
    half = lax.dynamic_slice_in_dim(pair_block, core_index * share, share, axis=1)
    sent = jnp.broadcast_to(half[None], (chips,) + half.shape)
    got = lax.all_to_all(sent, "chip", split_axis=0, concat_axis=0, tiled=True)
    got = got.reshape((chips * half.shape[0],) + half.shape[1:])
    low, high = core_swap(got)
    return jnp.concatenate([low, high], axis=1)


def quadratic_blocks(grid):
    vort, diverg, temper = jnp.split(grid, 3, axis=1)
    stacked = jnp.concatenate([vort * temper, diverg * temper, vort * diverg], axis=1)
    return stacked.astype(jnp.bfloat16)


def per_device(spectral, legendre, weights, nlon, assignment):
    wave_index = lax.axis_index("wave")
    lev_index = lax.axis_index("chip") * lax.axis_size("core") + lax.axis_index("core")
    slots = legendre.shape[0]
    lat_band = legendre.shape[1]
    kmax_width = legendre.shape[2]
    all_slots = assignment.shape[0]
    pairs_n = slots // 2
    own_waves = lax.dynamic_slice_in_dim(assignment, wave_index * slots, slots)
    krange = lax.iota(jnp.int32, kmax_width)
    front = krange[None, :] < (kmax_width - own_waves.reshape(pairs_n, 2)[:, 0])[:, None]
    leg_pairs = legendre.reshape(pairs_n, 2, lat_band, kmax_width)
    zero_bf = jnp.zeros((), jnp.bfloat16)
    leg_a = jnp.where(front[:, None, :], leg_pairs[:, 0], zero_bf)
    leg_b = jnp.where(front[:, None, :], zero_bf, leg_pairs[:, 1, :, ::-1])
    packed_leg = jnp.stack([leg_a, leg_b], axis=1)
    spec_pairs = spectral.reshape(spectral.shape[0], pairs_n, 2, kmax_width)
    packed_spec = jnp.where(front[None], spec_pairs[:, :, 0], spec_pairs[:, :, 1, ::-1])
    spec_all = chip_gather(packed_spec)
    columns = spec_all.shape[0]
    levels = columns // 6
    spec_split = spec_all.reshape(levels, 3, 2, pairs_n, kmax_width)
    four_local = jnp.einsum(
        "pxlk,vfrpk->pxlrfv", packed_leg, spec_split, preferred_element_type=jnp.float32
    ).astype(jnp.bfloat16).reshape(slots, lat_band, columns)
    fourier = lax.all_to_all(four_local, "wave", split_axis=1, concat_axis=0, tiled=True)
    mine = fourier.shape[1]
    half_cols = columns // 2
    lat_index = lev_index * lat_band + wave_index * mine + 0
    count = lax.dynamic_slice_in_dim(nlon, lat_index, 1)[0]
    weight = lax.dynamic_slice_in_dim(weights, lat_index, 1)[0]
    half_rows = NLONPAD // 2
    half = count // 2
    fine_rows = lax.iota(jnp.int32, 128)
    coarse_rows = lax.iota(jnp.int32, half_rows // 128) * 128
    lon_rows = lax.iota(jnp.int32, half_rows)
    fine_cos, fine_sin = angle_parts(count, assignment, fine_rows)
    coarse_cos, coarse_sin = angle_parts(count, assignment, coarse_rows)
    table = compose_table(
        half + 1, count, assignment, coarse_cos, coarse_sin, fine_cos, fine_sin, lon_rows
    )
    zero_bf = jnp.zeros((), jnp.bfloat16)
    blank = jnp.zeros((all_slots, half_cols), jnp.bfloat16)
    split = jnp.concatenate(
        [
            jnp.concatenate([fourier[:, 0, :half_cols], blank], axis=1),
            jnp.concatenate([blank, fourier[:, 0, half_cols:]], axis=1),
        ],
        axis=0,
    )
    parts = jnp.dot(table, split, preferred_element_type=jnp.float32)
    even, odd = parts[:, :half_cols], parts[:, half_cols:]
    grid_pos = 2.0 * (even + odd)
    grid_neg = 2.0 * (even - odd)
    mirrored = (lon_rows > 0) & (lon_rows < half)
    prod_pos = quadratic_blocks(grid_pos)
    prod_neg = jnp.where(mirrored[:, None], quadratic_blocks(grid_neg), zero_bf)
    both = jnp.concatenate([prod_pos, prod_neg], axis=1)
    total = lax.dot_general(
        table, both, (((0,), (0,)), ((), ())), preferred_element_type=jnp.float32
    )
    real = total[:all_slots, :half_cols] + total[:all_slots, half_cols:]
    imag = total[all_slots:, :half_cols] - total[all_slots:, half_cols:]
    scale = weight / count.astype(jnp.float32)
    joined = jnp.stack([real * scale, imag * scale], axis=-1).reshape(all_slots, 3, levels, 2)
    joined = jnp.transpose(joined, (0, 2, 1, 3)).reshape(all_slots, columns)
    analysed_rows = [joined.astype(jnp.bfloat16)]
    analysed = jnp.stack(analysed_rows, axis=1)
    returned = lax.all_to_all(analysed, "wave", split_axis=0, concat_axis=1, tiled=True)
    returned = returned.reshape(pairs_n, 2, lat_band, columns)
    band_term = jnp.einsum(
        "pxlc,pxlk->cpk", returned, packed_leg, preferred_element_type=jnp.float32
    )
    chips = lax.axis_size("chip")
    cores = lax.axis_size("core")
    core_index = lax.axis_index("core")
    shares = band_term.astype(jnp.bfloat16).reshape(
        chips, cores, columns // (chips * cores), pairs_n, kmax_width
    )
    keep = lax.dynamic_index_in_dim(shares, core_index, axis=1, keepdims=False)
    give = lax.dynamic_index_in_dim(shares, cores - 1 - core_index, axis=1, keepdims=False)
    got = lax.ppermute(give, "core", [(0, 1), (1, 0)])
    pair_sum = (keep.astype(jnp.float32) + got.astype(jnp.float32)).astype(jnp.bfloat16)
    gathered = lax.all_to_all(pair_sum, "chip", split_axis=0, concat_axis=0, tiled=True)
    summed = jnp.sum(gathered.astype(jnp.float32), axis=0)
    zero_f = jnp.zeros((), jnp.float32)
    out_a = jnp.where(front[None], summed, zero_f)
    out_b = jnp.where(front[None], zero_f, summed)[:, :, ::-1]
    out = jnp.stack([out_a, out_b], axis=2)
    return out.reshape(summed.shape[0], slots, kmax_width)


def solution(mesh):
    grid = mesh.devices.reshape(mesh.shape["wave"], mesh.shape["lev"] // 2, 2)
    split_mesh = jax.sharding.Mesh(grid, ("wave", "chip", "core"))
    return jax.shard_map(
        per_device,
        mesh=split_mesh,
        in_specs=(P(LEV, "wave", None), P("wave", LEV, None), P(), P(), P()),
        out_specs=P(LEV, "wave", None),
        check_vma=False,
    )
```
